512 devices in a mesh: src: 16 (over z_hi, x), dst: 32 (over z_lo, y, core).
Axes of the slice: x: 4, y: 4, z: 16 (z_hi: 4, z_lo: 4; z = z_hi * 4 + z_lo), core: 2. Of those that a mesh axis runs over, the one named last changes fastest.
Arguments:
- rel_ops: bfloat16 [2048, 400, 400], P(('src', 'dst')), may hold values from -0.3125 to 0.3125
- src_emb: bfloat16 [4096, 400], P('src'), may hold values from -1.796875 to 1.796875
- dst_emb: bfloat16 [8192, 400], P('dst'), may hold values from -6 to 6
- edge_src: int32 [16, 32, 1024], P('src', 'dst'), may hold values from 0 to 255
- edge_dst: int32 [16, 32, 1024], P('src', 'dst'), may hold values from 0 to 255
- slot_count: int32 [16, 32, 64], P('src', 'dst'), may hold values from 0 to 16, as said below
- neg_span: int32 [16, 2], P('src'), may hold values from 0 to 31
Outputs:
- grad_rel: bfloat16 [2048, 400, 400], P(('src', 'dst'))
- grad_src: bfloat16 [4096, 400], P('src')
- grad_dst: bfloat16 [8192, 400], P('dst')
The draws below stay inside these ranges and needn't reach their ends.
Inputs may be any that keep to these rules, and one draw needn't show every extreme that they name: Slot j of a bucket carries the relation given by its group as in the reference program; only the first slot_count slots of a group are live, and in every bucket some group has exactly 16 live slots.
All inputs are finite; a program needn't handle non-finite values.
Results may differ from the reference program's by a relative error of at most 0.015.
Values may be sent and summed in bfloat16 or wider, within the bound.
No kernel may reach another device: no remote copies, remote signals or barrier semaphores. Data moves between devices by JAX's collectives and lax.ppermute only.
A program may use at most 64 MiB of HBM per device.

```python
import jax
import jax.numpy as jnp
from jax import lax

D = 400
RD = 4
C = 16
PART = 256
NCH = 2
RELS = 2048
SLOTS = 1024
SRC_ENT = 4096
DST_ENT = 8192
N_SRC = 16
N_DST = 32


def draw_dst_emb(key, part):
    first = jax.random.fold_in(key, 0)
    row_total = N_DST * PART
    values = 0.3 * jax.random.normal(first, (row_total, D), jnp.float32)
    return jnp.clip(values, -6.0, 6.0).astype(jnp.bfloat16)


def draw_slot_count(key, part):
    first, second = jax.random.split(key)
    group_total = N_SRC * RD
    counts = jax.random.randint(first, (N_SRC, N_DST, group_total), 0, C + 1)
    full_group = jax.random.randint(second, (N_SRC, N_DST, 1), 0, group_total)
    groups = jnp.arange(group_total, dtype=jnp.int32)[None, None, :]
    return jnp.where(groups == full_group, C, counts).astype(jnp.int32)


def touch_ends(values, stream_key, smallest, top_value):
    shape = values.shape
    index_at = [jax.random.randint(jax.random.fold_in(stream_key, axis), (), 0, shape[axis]) for axis in range(len(shape))]
    values = values.at[tuple(index_at)].set(smallest)
    longest = shape.index(max(shape))
    index_at[longest] = (index_at[longest] + 1) % shape[longest]
    return values.at[tuple(index_at)].set(top_value)


def shard_levels(own_key, extent, pieces, low, largest):
    gain, own = 1.0, jax.random.fold_in(own_key, 6)
    for axis_at, shards_of in pieces:
        steps = jnp.exp(jax.random.uniform(jax.random.fold_in(own, axis_at), (shards_of,), jnp.float32, low / len(pieces), largest / len(pieces)))
        gain = gain * jnp.repeat(steps, extent[axis_at] // shards_of).reshape([-1 if axis == axis_at else 1 for axis in range(len(extent))])
    return gain


def normal_values(key, extent, deviation, bound, cuts=(), held_as=jnp.bfloat16):
    drawn = deviation * jax.random.normal(key, extent, jnp.float32)
    if cuts:
        drawn = drawn * shard_levels(key, extent, cuts, -0.22, 0.18)
    return jnp.clip(drawn, -bound, bound).astype(held_as)


def setup_inputs(seed: int = 0) -> dict:
    seeds = jax.random.split(jax.random.key(seed), 8)
    return {
        "rel_ops": normal_values(seeds[0], (RELS, D, D), D ** -0.5, 0.3125, ((0, 512),)),
        "src_emb": normal_values(seeds[1], (SRC_ENT, D), 0.3, 1.796875, ((0, 16),)),
        "dst_emb": draw_dst_emb(jax.random.fold_in(seeds[7], 71), 0),
        "edge_src": touch_ends(jax.random.randint(seeds[3], (N_SRC, N_DST, SLOTS), 0, PART), jax.random.fold_in(seeds[3], 1), 0, PART - 1).astype(jnp.int32),
        "edge_dst": touch_ends(jax.random.randint(seeds[4], (N_SRC, N_DST, SLOTS), 0, PART), jax.random.fold_in(seeds[4], 1), 0, PART - 1).astype(jnp.int32),
        "slot_count": draw_slot_count(jax.random.fold_in(seeds[7], 71), 0),
        "neg_span": touch_ends(jax.random.randint(seeds[6], (N_SRC, NCH), 0, N_DST), jax.random.fold_in(seeds[6], 1), 0, N_DST - 1).astype(jnp.int32),
    }


def bucket_terms(ops_col, x_part, y_part, negatives, ids_src, ids_dst, counts):
    slot_lane = jnp.arange(SLOTS, dtype=jnp.int32) % C
    slot_group = jnp.arange(SLOTS, dtype=jnp.int32) // C
    live_mask = (slot_lane < counts[slot_group]).astype(jnp.float32)
    inputs = x_part[ids_src].reshape(N_SRC, RD, C, D)
    mapped = jnp.einsum("okcd,okde->okce", inputs.astype(jnp.float32), ops_col.astype(jnp.float32))
    mapped = mapped.astype(jnp.bfloat16).reshape(SLOTS, D)
    targets = y_part[ids_dst]
    neg_score = jnp.dot(mapped, negatives.T, preferred_element_type=jnp.float32)
    pos_score = jnp.sum(mapped.astype(jnp.float32) * targets.astype(jnp.float32), -1)
    row_max = jnp.maximum(jnp.max(neg_score, -1), pos_score)
    exp_neg = jnp.exp(neg_score - row_max[:, None])
    exp_pos = jnp.exp(pos_score - row_max)
    denom = jnp.sum(exp_neg, -1) + exp_pos
    grad_neg = (exp_neg * (live_mask / denom)[:, None]).astype(jnp.bfloat16)
    grad_pos = (exp_pos / denom - 1.0) * live_mask
    upstream = grad_pos[:, None] * targets.astype(jnp.float32) + jnp.dot(grad_neg, negatives, preferred_element_type=jnp.float32)
    upstream = upstream.astype(jnp.bfloat16).reshape(N_SRC, RD, C, D)
    grad_ops = jnp.einsum("okcd,okce->okde", inputs.astype(jnp.float32), upstream.astype(jnp.float32))
    back_rows = jnp.einsum("okce,okde->okcd", upstream.astype(jnp.float32), ops_col.astype(jnp.float32))
    back_rows = back_rows.astype(jnp.bfloat16).reshape(SLOTS, D).astype(jnp.float32)
    src_term = jax.ops.segment_sum(back_rows, ids_src, num_segments=PART)
    dst_term = jax.ops.segment_sum(grad_pos[:, None] * mapped.astype(jnp.float32), ids_dst, num_segments=PART)
    span_term = jnp.dot(grad_neg.astype(jnp.float32).T, mapped.astype(jnp.float32))
    return grad_ops, src_term, dst_term, span_term


def add_rows(total, start, extra):
    start = start.astype(jnp.int32)
    current = lax.dynamic_slice_in_dim(total, start, extra.shape[0], 0)
    return lax.dynamic_update_slice_in_dim(total, current + extra, start, 0)


def reference(rel_ops, src_emb, dst_emb, edge_src, edge_dst, slot_count, neg_span):
    all_ops = rel_ops.reshape(N_SRC, N_DST, RD, D, D)

    def column(carry, dst_idx):
        grad_src_acc, grad_dst_acc = carry
        ops_col = lax.dynamic_index_in_dim(all_ops, dst_idx, 1, keepdims=False)
        y_part = lax.dynamic_slice_in_dim(dst_emb, (dst_idx * PART).astype(jnp.int32), PART, 0)

        def source(inner, src_idx):
            grad_ops, src_acc, dst_acc = inner
            x_part = lax.dynamic_slice_in_dim(src_emb, (src_idx * PART).astype(jnp.int32), PART, 0)
            span_ids = neg_span[src_idx]
            negatives = jnp.concatenate([lax.dynamic_slice_in_dim(dst_emb, (span_ids[index] * PART).astype(jnp.int32), PART, 0) for index in range(NCH)], 0)
            terms = bucket_terms(ops_col, x_part, y_part, negatives, edge_src[src_idx, dst_idx], edge_dst[src_idx, dst_idx], slot_count[src_idx, dst_idx])
            src_acc = add_rows(src_acc, src_idx * PART, terms[1])
            dst_acc = add_rows(dst_acc, dst_idx * PART, terms[2])
            for index in range(NCH):
                dst_acc = add_rows(dst_acc, span_ids[index] * PART, terms[3][index * PART:(index + 1) * PART])
            return (grad_ops + terms[0], src_acc, dst_acc), None

        start = (jnp.zeros((N_SRC, RD, D, D), jnp.float32), grad_src_acc, grad_dst_acc)
        (grad_ops, src_acc, dst_acc), _ = lax.scan(source, start, jnp.arange(N_SRC, dtype=jnp.int32))
        return (src_acc, dst_acc), grad_ops.astype(jnp.bfloat16)

    first = (jnp.zeros((SRC_ENT, D), jnp.float32), jnp.zeros((DST_ENT, D), jnp.float32))
    (grad_src, grad_dst), columns = lax.scan(column, first, jnp.arange(N_DST, dtype=jnp.int32))
    grad_rel = jnp.transpose(columns, (1, 0, 2, 3, 4)).reshape(RELS, D, D)
    return grad_rel, grad_src.astype(jnp.bfloat16), grad_dst.astype(jnp.bfloat16)
```

```python
import jax
import jax.numpy as jnp
from jax import lax
from jax.sharding import PartitionSpec as P

F32 = jnp.float32
BF16 = jnp.bfloat16


def butterfly_sum(x, axis, bits):
    n = lax.axis_size(axis)
    for bit in bits:
        low = x.astype(BF16)
        other = lax.ppermute(low, axis, [(i, i ^ bit) for i in range(n)])
        x = low.astype(F32) + other.astype(F32)
    return x


def axis_bits(n):
    return [1 << b for b in range(n.bit_length() - 1)]


def softmax_grads(z, y, negs, live):
    neg = jnp.einsum("...md,...nd->...mn", z, negs, preferred_element_type=F32)
    pos = jnp.sum(z.astype(F32) * y.astype(F32), -1)
    row_max = jnp.maximum(jnp.max(neg, -1), pos)
    exp_neg = jnp.exp(neg - row_max[..., None])
    exp_pos = jnp.exp(pos - row_max)
    denom = jnp.sum(exp_neg, -1) + exp_pos
    g_neg = (exp_neg * (live / denom)[..., None]).astype(BF16)
    g_pos = (exp_pos / denom - 1.0) * live
    return g_neg, g_pos


def body(rel_ops, src_emb, dst_emb, edge_src, edge_dst, slot_count, neg_span):
    n_src = lax.axis_size("src")
    n_dst = lax.axis_size("dst")
    rk = rel_ops.shape[0]
    width = rel_ops.shape[1]
    part = src_emb.shape[0]
    slots = edge_src.shape[2]
    cap = slots // (n_src * rk)
    nch = neg_span.shape[1]
    group = rk * cap
    ids_src = edge_src.reshape(slots)
    ids_dst = edge_dst.reshape(slots)
    counts = slot_count.reshape(n_src * rk)
    spans = neg_span.reshape(nch)
    own_dst = lax.axis_index("dst")

    every_dst = lax.all_gather(dst_emb, "dst", tiled=False)

    meta = jnp.concatenate(
        [
            jnp.broadcast_to(spans[None, :], (n_src, nch)),
            counts.reshape(n_src, rk),
            ids_dst.reshape(n_src, group),
        ],
        axis=1,
    ).astype(BF16)
    meta = jnp.pad(meta, ((0, 0), (0, width - meta.shape[1])))
    inputs = src_emb[ids_src].reshape(n_src, group, width)
    payload = jnp.concatenate([inputs, meta[:, None, :]], axis=1)
    received = lax.all_to_all(payload, "src", 0, 0, tiled=True)

    x_in = received[:, :group, :].reshape(n_src, rk, cap, width)
    info = received[:, group, :].astype(F32)
    span_in = info[:, :nch].astype(jnp.int32)
    count_in = info[:, nch : nch + rk]
    dst_in = info[:, nch + rk : nch + rk + group].astype(jnp.int32)
    mapped = jnp.einsum(
        "pkcd,kde->pkce", x_in, rel_ops, preferred_element_type=F32
    ).astype(BF16)
    mapped_back = lax.all_to_all(mapped, "src", 0, 0, tiled=True)

    z_in = mapped.reshape(n_src, group, width)
    y_in = dst_emb[dst_in.reshape(-1)].reshape(n_src, group, width)
    negs_in = every_dst[span_in].reshape(n_src, nch * part, width)
    lane = jnp.arange(cap, dtype=F32)
    live_in = (lane[None, None, :] < count_in[:, :, None]).astype(F32).reshape(n_src, group)
    g_neg, g_pos = softmax_grads(z_in, y_in, negs_in, live_in)
    upstream = (
        g_pos[..., None] * y_in.astype(F32)
        + jnp.einsum("pmn,pnd->pmd", g_neg, negs_in, preferred_element_type=F32)
    ).astype(BF16)
    upstream = upstream.reshape(n_src, rk, cap, width)
    grad_rel = jnp.einsum(
        "pkcd,pkce->kde", x_in, upstream, preferred_element_type=F32
    ).astype(BF16)
    back_rows = jnp.einsum(
        "pkce,kde->pkcd", upstream, rel_ops, preferred_element_type=F32
    ).astype(BF16)
    back_rows = lax.all_to_all(back_rows, "src", 0, 0, tiled=True)

    src_local = jax.ops.segment_sum(
        back_rows.reshape(slots, width).astype(F32), ids_src, num_segments=part
    )
    grad_src = butterfly_sum(src_local, "dst", axis_bits(n_dst)).astype(BF16)

    z_b = mapped_back.reshape(slots, width)
    y_b = dst_emb[ids_dst]
    negs = every_dst[spans].reshape(nch * part, width)
    slot_lane = jnp.arange(slots, dtype=jnp.int32) % cap
    live = (
        slot_lane < jnp.repeat(counts, cap, total_repeat_length=slots)
    ).astype(F32)
    g_neg_b, g_pos_b = softmax_grads(z_b, y_b, negs, live)
    dst_local = jax.ops.segment_sum(
        g_pos_b[:, None] * z_b.astype(F32), ids_dst, num_segments=part
    )
    span_grad = jnp.einsum("bn,bd->nd", g_neg_b, z_b, preferred_element_type=F32)
    span_sum = butterfly_sum(span_grad, "dst", axis_bits(n_dst))
    for index in range(nch):
        piece = span_sum[index * part : (index + 1) * part]
        dst_local = dst_local + jnp.where(spans[index] == own_dst, piece, 0.0)
    grad_dst = butterfly_sum(dst_local, "src", axis_bits(n_src)).astype(BF16)
    return (grad_rel, grad_src, grad_dst)


def solution(mesh):
    placed = (
        P(("src", "dst"), None, None),
        P("src", None),
        P("dst", None),
        P("src", "dst", None),
        P("src", "dst", None),
        P("src", "dst", None),
        P("src", None),
    )
    return jax.shard_map(
        body,
        mesh=mesh,
        in_specs=placed,
        out_specs=(P(("src", "dst"), None, None), P("src", None), P("dst", None)),
        check_vma=False,
    )
```

```python
import jax
import jax.numpy as jnp
from jax import lax
from jax.sharding import PartitionSpec as P

F32 = jnp.float32
BF16 = jnp.bfloat16


def butterfly_sum(x, axis, bits):
    n = lax.axis_size(axis)
    for bit in bits:
        low = x.astype(BF16)
        other = lax.ppermute(low, axis, [(i, i ^ bit) for i in range(n)])
        x = low.astype(F32) + other.astype(F32)
    return x


def axis_bits(n):
    return [1 << b for b in range(n.bit_length() - 1)]


def group_round(x, axis, stride, size):
    n = lax.axis_size(axis)
    me = lax.axis_index(axis)
    member = (me // stride) % size
    low = x.astype(BF16)
    got = [low]
    for shift in range(1, size):
        perm = []
        for i in range(n):
            m = (i // stride) % size
            perm.append((i, i + (((m + shift) % size) - m) * stride))
        got.append(lax.ppermute(low, axis, perm))
    stacked = jnp.stack(got)
    order = (member - jnp.arange(size)) % size
    ordered = stacked[order].astype(F32)
    total = ordered[0]
    for j in range(1, size):
        total = total + ordered[j]
    return total


def sub_axes(n):
    shapes = {32: ((1, 2), (2, 4), (8, 4)), 16: ((1, 4), (4, 4))}
    return shapes.get(n)


def axis_sum(x, axis):
    n = lax.axis_size(axis)
    parts = sub_axes(n)
    if parts is None:
        return butterfly_sum(x, axis, axis_bits(n))
    for stride, size in parts:
        x = group_round(x, axis, stride, size)
    return x


def softmax_grads(z, y, negs, live):
    neg = jnp.einsum("...md,...nd->...mn", z, negs, preferred_element_type=F32)
    pos = jnp.sum(z.astype(F32) * y.astype(F32), -1)
    row_max = jnp.maximum(jnp.max(neg, -1), pos)
    exp_neg = jnp.exp(neg - row_max[..., None])
    exp_pos = jnp.exp(pos - row_max)
    denom = jnp.sum(exp_neg, -1) + exp_pos
    g_neg = (exp_neg * (live / denom)[..., None]).astype(BF16)
    g_pos = (exp_pos / denom - 1.0) * live
    return g_neg, g_pos


def body(rel_ops, src_emb, dst_emb, edge_src, edge_dst, slot_count, neg_span):
    n_src = lax.axis_size("src")
    n_dst = lax.axis_size("dst")
    rk = rel_ops.shape[0]
    width = rel_ops.shape[1]
    part = src_emb.shape[0]
    slots = edge_src.shape[2]
    cap = slots // (n_src * rk)
    nch = neg_span.shape[1]
    group = rk * cap
    ids_src = edge_src.reshape(slots)
    ids_dst = edge_dst.reshape(slots)
    counts = slot_count.reshape(n_src * rk)
    spans = neg_span.reshape(nch)
    own_dst = lax.axis_index("dst")

    every_dst = lax.all_gather(dst_emb, "dst", tiled=False)

    meta = jnp.concatenate(
        [
            jnp.broadcast_to(spans[None, :], (n_src, nch)),
            counts.reshape(n_src, rk),
            ids_dst.reshape(n_src, group),
        ],
        axis=1,
    ).astype(BF16)
    meta = jnp.pad(meta, ((0, 0), (0, width - meta.shape[1])))
    inputs = src_emb[ids_src].reshape(n_src, group, width)
    payload = jnp.concatenate([inputs, meta[:, None, :]], axis=1)
    received = lax.all_to_all(payload, "src", 0, 0, tiled=True)

    x_in = received[:, :group, :].reshape(n_src, rk, cap, width)
    info = received[:, group, :].astype(F32)
    span_in = info[:, :nch].astype(jnp.int32)
    count_in = info[:, nch : nch + rk]
    dst_in = info[:, nch + rk : nch + rk + group].astype(jnp.int32)
    mapped = jnp.einsum(
        "pkcd,kde->pkce", x_in, rel_ops, preferred_element_type=F32
    ).astype(BF16)
    mapped_back = lax.all_to_all(mapped, "src", 0, 0, tiled=True)

    z_in = mapped.reshape(n_src, group, width)
    y_in = dst_emb[dst_in.reshape(-1)].reshape(n_src, group, width)
    negs_in = every_dst[span_in].reshape(n_src, nch * part, width)
    lane = jnp.arange(cap, dtype=F32)
    live_in = (lane[None, None, :] < count_in[:, :, None]).astype(F32).reshape(n_src, group)
    g_neg, g_pos = softmax_grads(z_in, y_in, negs_in, live_in)
    upstream = (
        g_pos[..., None] * y_in.astype(F32)
        + jnp.einsum("pmn,pnd->pmd", g_neg, negs_in, preferred_element_type=F32)
    ).astype(BF16)
    upstream = upstream.reshape(n_src, rk, cap, width)
    grad_rel = jnp.einsum(
        "pkcd,pkce->kde", x_in, upstream, preferred_element_type=F32
    ).astype(BF16)
    back_rows = jnp.einsum(
        "pkce,kde->pkcd", upstream, rel_ops, preferred_element_type=F32
    ).astype(BF16)
    back_rows = lax.all_to_all(back_rows, "src", 0, 0, tiled=True)

    src_local = jax.ops.segment_sum(
        back_rows.reshape(slots, width).astype(F32), ids_src, num_segments=part
    )

    z_b = mapped_back.reshape(slots, width)
    y_b = dst_emb[ids_dst]
    negs = every_dst[spans].reshape(nch * part, width)
    slot_lane = jnp.arange(slots, dtype=jnp.int32) % cap
    live = (
        slot_lane < jnp.repeat(counts, cap, total_repeat_length=slots)
    ).astype(F32)
    g_neg_b, g_pos_b = softmax_grads(z_b, y_b, negs, live)
    dst_local = jax.ops.segment_sum(
        g_pos_b[:, None] * z_b.astype(F32), ids_dst, num_segments=part
    )
    span_grad = jnp.einsum("bn,bd->nd", g_neg_b, z_b, preferred_element_type=F32)
    joint = axis_sum(jnp.concatenate([src_local, span_grad], 0), "dst")
    grad_src = joint[:part].astype(BF16)
    span_sum = joint[part:]
    for index in range(nch):
        piece = span_sum[index * part : (index + 1) * part]
        dst_local = dst_local + jnp.where(spans[index] == own_dst, piece, 0.0)
    grad_dst = axis_sum(dst_local, "src").astype(BF16)
    return (grad_rel, grad_src, grad_dst)


def solution(mesh):
    placed = (
        P(("src", "dst"), None, None),
        P("src", None),
        P("dst", None),
        P("src", "dst", None),
        P("src", "dst", None),
        P("src", "dst", None),
        P("src", None),
    )
    return jax.shard_map(
        body,
        mesh=mesh,
        in_specs=placed,
        out_specs=(P(("src", "dst"), None, None), P("src", None), P("dst", None)),
        check_vma=False,
    )
```

```python
import jax
import jax.numpy as jnp
from jax import lax
from jax.sharding import PartitionSpec as P

F32 = jnp.float32
BF16 = jnp.bfloat16


def butterfly_sum(x, axis, bits):
    n = lax.axis_size(axis)
    for bit in bits:
        low = x.astype(BF16)
        other = lax.ppermute(low, axis, [(i, i ^ bit) for i in range(n)])
        x = low.astype(F32) + other.astype(F32)
    return x


def axis_bits(n):
    return [1 << b for b in range(n.bit_length() - 1)]


def group_round(x, axis, stride, size):
    n = lax.axis_size(axis)
    me = lax.axis_index(axis)
    member = (me // stride) % size
    low = x.astype(BF16)
    got = [low]
    for shift in range(1, size):
        perm = []
        for i in range(n):
            m = (i // stride) % size
            perm.append((i, i + (((m + shift) % size) - m) * stride))
        got.append(lax.ppermute(low, axis, perm))
    stacked = jnp.stack(got)
    order = (member - jnp.arange(size)) % size
    ordered = stacked[order].astype(F32)
    total = ordered[0]
    for j in range(1, size):
        total = total + ordered[j]
    return total


def sub_axes(n):
    shapes = {32: ((1, 2), (2, 4), (8, 4)), 16: ((1, 4), (4, 4))}
    return shapes.get(n)


def axis_sum(x, axis):
    n = lax.axis_size(axis)
    parts = sub_axes(n)
    if parts is None:
        return butterfly_sum(x, axis, axis_bits(n))
    for stride, size in parts:
        x = group_round(x, axis, stride, size)
    return x


def softmax_grads(z, y, negs, live):
    neg = jnp.einsum("...md,...nd->...mn", z, negs, preferred_element_type=F32)
    pos = jnp.sum(z.astype(F32) * y.astype(F32), -1)
    row_max = jnp.maximum(jnp.max(neg, -1), pos)
    exp_neg = jnp.exp(neg - row_max[..., None])
    exp_pos = jnp.exp(pos - row_max)
    denom = jnp.sum(exp_neg, -1) + exp_pos
    g_neg = (exp_neg * (live / denom)[..., None]).astype(BF16)
    g_pos = (exp_pos / denom - 1.0) * live
    return g_neg, g_pos


def body(rel_ops, src_emb, dst_emb, edge_src, edge_dst, slot_count, neg_span):
    n_src = lax.axis_size("src")
    n_dst = lax.axis_size("dst")
    rk = rel_ops.shape[0]
    width = rel_ops.shape[1]
    part = src_emb.shape[0]
    slots = edge_src.shape[2]
    cap = slots // (n_src * rk)
    nch = neg_span.shape[1]
    ids_src = edge_src.reshape(slots)
    ids_dst = edge_dst.reshape(slots)
    counts = slot_count.reshape(n_src * rk)
    spans = neg_span.reshape(nch)
    own_dst = lax.axis_index("dst")
    dst_bits = axis_bits(n_dst)

    pieces = jnp.stack(
        [jnp.where(spans[i] == own_dst, dst_emb, jnp.zeros_like(dst_emb)) for i in range(nch)]
    )
    negs = butterfly_sum(pieces, "dst", dst_bits).astype(BF16).reshape(nch * part, width)

    inputs = src_emb[ids_src].reshape(n_src, rk, cap, width)
    x_in = lax.all_to_all(inputs, "src", 0, 0, tiled=True)
    mapped = jnp.einsum(
        "pkcd,kde->pkce", x_in, rel_ops, preferred_element_type=F32
    ).astype(BF16)
    z_b = lax.all_to_all(mapped, "src", 0, 0, tiled=True).reshape(slots, width)

    y_b = dst_emb[ids_dst]
    lane = jnp.arange(cap, dtype=jnp.int32)
    live = (lane[None, :] < counts[:, None]).astype(F32).reshape(slots)
    g_neg, g_pos = softmax_grads(z_b, y_b, negs, live)
    upstream = (
        g_pos[:, None] * y_b.astype(F32)
        + jnp.dot(g_neg, negs, preferred_element_type=F32)
    ).astype(BF16)
    u_in = lax.all_to_all(
        upstream.reshape(n_src, rk, cap, width), "src", 0, 0, tiled=True
    )
    grad_rel = jnp.einsum(
        "pkcd,pkce->kde", x_in, u_in, preferred_element_type=F32
    ).astype(BF16)
    back_rows = jnp.einsum(
        "pkce,kde->pkcd", u_in, rel_ops, preferred_element_type=F32
    ).astype(BF16)
    back_rows = lax.all_to_all(back_rows, "src", 0, 0, tiled=True)

    dst_local = jax.ops.segment_sum(
        g_pos[:, None] * z_b.astype(F32), ids_dst, num_segments=part
    )
    span_grad = jnp.einsum("bn,bd->nd", g_neg, z_b, preferred_element_type=F32)
    span_sum = butterfly_sum(span_grad, "dst", dst_bits)
    for index in range(nch):
        piece = span_sum[index * part : (index + 1) * part]
        dst_local = dst_local + jnp.where(spans[index] == own_dst, piece, 0.0)
    grad_dst = butterfly_sum(dst_local, "src", axis_bits(n_src)).astype(BF16)

    src_local = jax.ops.segment_sum(
        back_rows.reshape(slots, width).astype(F32), ids_src, num_segments=part
    )
    grad_src = butterfly_sum(src_local, "dst", dst_bits).astype(BF16)
    return (grad_rel, grad_src, grad_dst)


def solution(mesh):
    placed = (
        P(("src", "dst"), None, None),
        P("src", None),
        P("dst", None),
        P("src", "dst", None),
        P("src", "dst", None),
        P("src", "dst", None),
        P("src", None),
    )
    return jax.shard_map(
        body,
        mesh=mesh,
        in_specs=placed,
        out_specs=(P(("src", "dst"), None, None), P("src", None), P("dst", None)),
        check_vma=False,
    )
```

```python
import jax
import jax.numpy as jnp
from jax import lax
from jax.sharding import PartitionSpec as P

F32 = jnp.float32
BF16 = jnp.bfloat16


def butterfly_sum(x, axis, bits):
    n = lax.axis_size(axis)
    for bit in bits:
        low = x.astype(BF16)
        other = lax.ppermute(low, axis, [(i, i ^ bit) for i in range(n)])
        x = low.astype(F32) + other.astype(F32)
    return x


def axis_bits(n):
    return [1 << b for b in range(n.bit_length() - 1)]


def softmax_grads(z, y, negs, live):
    neg = jnp.einsum("...md,...nd->...mn", z, negs, preferred_element_type=F32)
    pos = jnp.sum(z.astype(F32) * y.astype(F32), -1)
    row_max = jnp.maximum(jnp.max(neg, -1), pos)
    exp_neg = jnp.exp(neg - row_max[..., None])
    exp_pos = jnp.exp(pos - row_max)
    denom = jnp.sum(exp_neg, -1) + exp_pos
    g_neg = (exp_neg * (live / denom)[..., None]).astype(BF16)
    g_pos = (exp_pos / denom - 1.0) * live
    return g_neg, g_pos


def body(rel_ops, src_emb, dst_emb, edge_src, edge_dst, slot_count, neg_span):
    n_src = lax.axis_size("src")
    n_dst = lax.axis_size("dst")
    rk = rel_ops.shape[0]
    width = rel_ops.shape[1]
    part = src_emb.shape[0]
    slots = edge_src.shape[2]
    cap = slots // (n_src * rk)
    nch = neg_span.shape[1]
    ids_src = edge_src.reshape(slots)
    ids_dst = edge_dst.reshape(slots)
    counts = slot_count.reshape(n_src * rk)
    spans = neg_span.reshape(nch)
    own_dst = lax.axis_index("dst")
    dst_bits = axis_bits(n_dst)

    pieces = jnp.stack(
        [jnp.where(spans[i] == own_dst, dst_emb, jnp.zeros_like(dst_emb)) for i in range(nch)]
    )
    negs = butterfly_sum(pieces, "dst", dst_bits).astype(BF16).reshape(nch * part, width)

    inputs = src_emb[ids_src].reshape(n_src, rk, cap, width)
    x_in = lax.all_to_all(inputs, "src", 0, 0, tiled=True)
    mapped = jnp.einsum(
        "pkcd,kde->pkce", x_in, rel_ops, preferred_element_type=F32
    ).astype(BF16)
    z_b = lax.all_to_all(mapped, "src", 0, 0, tiled=True).reshape(slots, width)

    y_b = dst_emb[ids_dst]
    lane = jnp.arange(cap, dtype=jnp.int32)
    live = (lane[None, :] < counts[:, None]).astype(F32).reshape(slots)
    g_neg, g_pos = softmax_grads(z_b, y_b, negs, live)
    upstream = (
        g_pos[:, None] * y_b.astype(F32)
        + jnp.dot(g_neg, negs, preferred_element_type=F32)
    ).astype(BF16)
    u_in = lax.all_to_all(
        upstream.reshape(n_src, rk, cap, width), "src", 0, 0, tiled=True
    )
    grad_rel = jnp.einsum(
        "pkcd,pkce->kde", x_in, u_in, preferred_element_type=F32
    ).astype(BF16)
    back_rows = jnp.einsum(
        "pkce,kde->pkcd", u_in, rel_ops, preferred_element_type=F32
    ).astype(BF16)
    back_rows = lax.all_to_all(back_rows, "src", 0, 0, tiled=True)

    rows = jnp.arange(part, dtype=jnp.int32)[:, None]
    to_dst = jnp.where(ids_dst[None, :] == rows, g_pos[None, :], 0.0)
    dst_local = jnp.dot(
        to_dst, z_b.astype(F32), precision=lax.Precision.HIGHEST,
        preferred_element_type=F32,
    )
    span_grad = jnp.einsum("bn,bd->nd", g_neg, z_b, preferred_element_type=F32)
    span_sum = butterfly_sum(span_grad, "dst", dst_bits)
    for index in range(nch):
        piece = span_sum[index * part : (index + 1) * part]
        dst_local = dst_local + jnp.where(spans[index] == own_dst, piece, 0.0)
    grad_dst = butterfly_sum(dst_local, "src", axis_bits(n_src)).astype(BF16)

    to_src = (ids_src[None, :] == rows).astype(BF16)
    src_local = jnp.dot(
        to_src, back_rows.reshape(slots, width), preferred_element_type=F32
    )
    grad_src = butterfly_sum(src_local, "dst", dst_bits).astype(BF16)
    return (grad_rel, grad_src, grad_dst)


def solution(mesh):
    placed = (
        P(("src", "dst"), None, None),
        P("src", None),
        P("dst", None),
        P("src", "dst", None),
        P("src", "dst", None),
        P("src", "dst", None),
        P("src", None),
    )
    return jax.shard_map(
        body,
        mesh=mesh,
        in_specs=placed,
        out_specs=(P(("src", "dst"), None, None), P("src", None), P("dst", None)),
        check_vma=False,
    )
```

```python
import jax
import jax.numpy as jnp
from jax import lax
from jax.sharding import PartitionSpec as P

F32 = jnp.float32
BF16 = jnp.bfloat16


def butterfly_sum(x, axis, bits):
    n = lax.axis_size(axis)
    shape = x.shape
    x = lanes(x)
    for bit in bits:
        low = x.astype(BF16)
        other = lax.ppermute(low, axis, [(i, i ^ bit) for i in range(n)])
        x = low.astype(F32) + other.astype(F32)
    return x.reshape(shape)


def lanes(x):
    return x.reshape(-1, 128) if x.size % 128 == 0 else x


def exchange(x, axis):
    shape = x.shape
    flat = x.reshape(shape[0], -1)
    return lax.all_to_all(flat, axis, 0, 0, tiled=True).reshape(shape)


def axis_bits(n):
    return [1 << b for b in range(n.bit_length() - 1)]


def softmax_grads(z, y, negs, live):
    neg = jnp.einsum("...md,...nd->...mn", z, negs, preferred_element_type=F32)
    pos = jnp.sum(z.astype(F32) * y.astype(F32), -1)
    row_max = jnp.maximum(jnp.max(neg, -1), pos)
    exp_neg = jnp.exp(neg - row_max[..., None])
    exp_pos = jnp.exp(pos - row_max)
    denom = jnp.sum(exp_neg, -1) + exp_pos
    g_neg = (exp_neg * (live / denom)[..., None]).astype(BF16)
    g_pos = (exp_pos / denom - 1.0) * live
    return g_neg, g_pos


def body(rel_ops, src_emb, dst_emb, edge_src, edge_dst, slot_count, neg_span):
    n_src = lax.axis_size("src")
    n_dst = lax.axis_size("dst")
    rk = rel_ops.shape[0]
    width = rel_ops.shape[1]
    part = src_emb.shape[0]
    slots = edge_src.shape[2]
    cap = slots // (n_src * rk)
    nch = neg_span.shape[1]
    ids_src = edge_src.reshape(slots)
    ids_dst = edge_dst.reshape(slots)
    counts = slot_count.reshape(n_src * rk)
    spans = neg_span.reshape(nch)
    own_dst = lax.axis_index("dst")
    dst_bits = axis_bits(n_dst)

    pieces = jnp.stack(
        [jnp.where(spans[i] == own_dst, dst_emb, jnp.zeros_like(dst_emb)) for i in range(nch)]
    )
    negs = butterfly_sum(pieces, "dst", dst_bits).astype(BF16).reshape(nch * part, width)

    inputs = src_emb[ids_src].reshape(n_src, rk, cap, width)
    x_in = exchange(inputs, "src")
    mapped = jnp.einsum(
        "pkcd,kde->pkce", x_in, rel_ops, preferred_element_type=F32
    ).astype(BF16)
    z_b = exchange(mapped, "src").reshape(slots, width)

    y_b = dst_emb[ids_dst]
    lane = jnp.arange(cap, dtype=jnp.int32)
    live = (lane[None, :] < counts[:, None]).astype(F32).reshape(slots)
    g_neg, g_pos = softmax_grads(z_b, y_b, negs, live)
    upstream = (
        g_pos[:, None] * y_b.astype(F32)
        + jnp.dot(g_neg, negs, preferred_element_type=F32)
    ).astype(BF16)
    u_in = exchange(upstream.reshape(n_src, rk, cap, width), "src")
    grad_rel = jnp.einsum(
        "pkcd,pkce->kde", x_in, u_in, preferred_element_type=F32
    ).astype(BF16)
    back_rows = jnp.einsum(
        "pkce,kde->pkcd", u_in, rel_ops, preferred_element_type=F32
    ).astype(BF16)
    back_rows = exchange(back_rows, "src")

    rows = jnp.arange(part, dtype=jnp.int32)[:, None]
    to_dst = jnp.where(ids_dst[None, :] == rows, g_pos[None, :], 0.0)
    dst_local = jnp.dot(
        to_dst, z_b.astype(F32), precision=lax.Precision.HIGHEST,
        preferred_element_type=F32,
    )
    span_grad = jnp.einsum("bn,bd->nd", g_neg, z_b, preferred_element_type=F32)
    span_sum = butterfly_sum(span_grad, "dst", dst_bits)
    for index in range(nch):
        piece = span_sum[index * part : (index + 1) * part]
        dst_local = dst_local + jnp.where(spans[index] == own_dst, piece, 0.0)
    grad_dst = butterfly_sum(dst_local, "src", axis_bits(n_src)).astype(BF16)

    to_src = (ids_src[None, :] == rows).astype(BF16)
    src_local = jnp.dot(
        to_src, back_rows.reshape(slots, width), preferred_element_type=F32
    )
    grad_src = butterfly_sum(src_local, "dst", dst_bits).astype(BF16)
    return (grad_rel, grad_src, grad_dst)


def solution(mesh):
    placed = (
        P(("src", "dst"), None, None),
        P("src", None),
        P("dst", None),
        P("src", "dst", None),
        P("src", "dst", None),
        P("src", "dst", None),
        P("src", None),
    )
    return jax.shard_map(
        body,
        mesh=mesh,
        in_specs=placed,
        out_specs=(P(("src", "dst"), None, None), P("src", None), P("dst", None)),
        check_vma=False,
    )
```
